256 devices in a mesh: joint: 8 (over z), frame: 32 (over y, x, core).
Axes of the slice: x: 4, y: 4, z: 8, core: 2. Of those that a mesh axis runs over, the one named last changes fastest.
Arguments:
- tokens: bfloat16 [64, 768, 1536], P('joint', 'frame'), may hold values from -500 to 500
- norm_gain: float32 [1536], replicated, may hold values from 0.1 to 1.9
- qkv_weight: bfloat16 [1536, 3072], P('frame'), may hold values from -3 to 3
- out_grad: bfloat16 [64, 768, 1024], P('joint', 'frame'), may hold values from -6 to 6
Outputs:
- attended: bfloat16 [64, 768, 1024], P('joint', 'frame')
- token_grad: bfloat16 [64, 768, 1536], P('joint', 'frame')
- weight_grad: float32 [1536, 3072], P('frame')
- gain_grad: float32 [1536], replicated
The draws below stay inside these ranges and needn't reach their ends.
All inputs are finite; a program needn't handle non-finite values.
Results may differ from the reference program's by a relative error of at most 0.029.
The reference program's roundings to bfloat16 on the way (of `scaled`, `projected`, `probs_low`, `score_grad`, `query_grad` and `qkv_grad`) count: a program that leaves them out, or rounds other values in their place, can miss the bound.
Values may be sent and summed in bfloat16 or wider, within the bound.
No kernel may reach another device: no remote copies, remote signals or barrier semaphores. Data moves between devices by JAX's collectives and lax.ppermute only.
A program may use at most 128 MiB of HBM per device.

```python
import jax
import jax.numpy as jnp
from jax import lax

D = 1536
HEADS = 8
HDIM = 128
JOINTS = 64
HD = 1024
FRAMES = 768
N_JOINT = 8
N_FRAME = 32


def draw_tokens(key, part):
    first = jax.random.fold_in(key, 0)
    base = jnp.clip(jax.random.normal(first, (JOINTS, FRAMES, D), jnp.float32), -4.0, 4.0)
    return base.astype(jnp.bfloat16)


def draw_qkv_weight(key, part):
    inner = HEADS * HDIM
    base = jnp.clip(jax.random.normal(key, (D, 3 * inner), jnp.float32), -4.0, 4.0) / jnp.sqrt(jnp.float32(D))
    return jnp.clip(base, -3.0, 3.0).astype(jnp.bfloat16)


def shard_levels(key, dims, shards, least, largest):
    def one(position, shards_of):
        heights = jax.random.uniform(jax.random.fold_in(jax.random.fold_in(key, 6), position), (shards_of,), jnp.float32, least / len(shards), largest / len(shards))
        return jnp.repeat(jnp.exp(heights), dims[position] // shards_of).reshape((-1,) + (1,) * (len(dims) - position - 1))

    gain = one(*shards[0])
    for cut in shards[1:]:
        gain = gain * one(*cut)
    return gain


def bell_draw(key, dims, scale, most, cuts=(), dtype=jnp.bfloat16):
    entries = jax.random.normal(key, dims, jnp.float32) * scale
    if len(cuts) > 0:
        entries = shard_levels(key, dims, cuts, -0.22, 0.18) * entries
    return jnp.clip(entries, min=-most, max=most).astype(dtype)


def setup_inputs(seed: int = 0) -> dict:
    key_list = jax.random.split(jax.random.key(seed), 5)
    return {
        "tokens": draw_tokens(jax.random.fold_in(key_list[4], 71), 0),
        "norm_gain": jnp.clip(1.0 + 0.18 * jax.random.normal(key_list[1], (D,), jnp.float32), 0.1, 1.9),
        "qkv_weight": draw_qkv_weight(jax.random.fold_in(key_list[4], 71), 0),
        "out_grad": bell_draw(key_list[3], (JOINTS, FRAMES, HD), 1.0, 6.0, ((0, 8), (1, 32))),
    }


EPSILON = 1e-05

def reference(tokens, norm_gain, qkv_weight, out_grad):
    hd = HEADS * HDIM
    flat = tokens.astype(jnp.float32)
    rinv = lax.rsqrt(lax.optimization_barrier(jnp.mean(flat * flat, axis=-1, keepdims=True)) + EPSILON)
    normed = flat * rinv
    gain32 = norm_gain.astype(jnp.float32)
    scaled = (normed * gain32).astype(jnp.bfloat16)
    scaled_rows = scaled.reshape(JOINTS * FRAMES, D)
    projected = jnp.dot(scaled_rows, qkv_weight, preferred_element_type=jnp.float32).astype(jnp.bfloat16)
    projected = projected.reshape(JOINTS, FRAMES, 3, HEADS, HDIM).astype(jnp.float32)
    queries = projected[:, :, 0]
    keys_all = projected[:, :, 1]
    values_all = projected[:, :, 2]
    inv_root = 1.0 / HDIM ** 0.5
    scores = jnp.einsum('ifhd,jfhd->fhij', queries, keys_all) * inv_root
    probs = jax.nn.softmax(scores, axis=-1)
    probs_low = probs.astype(jnp.bfloat16).astype(jnp.float32)
    attended = jnp.einsum('fhij,jfhd->ifhd', probs_low, values_all).astype(jnp.bfloat16)
    attended = attended.reshape(JOINTS, FRAMES, hd)
    upstream = out_grad.astype(jnp.float32).reshape(JOINTS, FRAMES, HEADS, HDIM)
    prob_grad = jnp.einsum('ifhd,jfhd->fhij', upstream, values_all)
    carried = lax.optimization_barrier(jnp.sum(probs * prob_grad, axis=-1, keepdims=True))
    score_grad = (probs * (prob_grad - carried) * inv_root).astype(jnp.bfloat16).astype(jnp.float32)
    query_grad = jnp.einsum('fhij,jfhd->ifhd', score_grad, keys_all).astype(jnp.bfloat16)
    group = JOINTS // N_JOINT
    key_total = jnp.zeros((JOINTS, FRAMES, HEADS, HDIM), jnp.float32)
    value_total = jnp.zeros((JOINTS, FRAMES, HEADS, HDIM), jnp.float32)
    for index in range(N_JOINT):
        low = index * group
        score_piece = score_grad[:, :, low:low + group, :]
        prob_piece = probs_low[:, :, low:low + group, :]
        key_piece = jnp.einsum('fhij,ifhd->jfhd', score_piece, queries[low:low + group])
        value_piece = jnp.einsum('fhij,ifhd->jfhd', prob_piece, upstream[low:low + group])
        key_total = key_total + key_piece.astype(jnp.bfloat16).astype(jnp.float32)
        value_total = value_total + value_piece.astype(jnp.bfloat16).astype(jnp.float32)
    key_grad = key_total.astype(jnp.bfloat16)
    value_grad = value_total.astype(jnp.bfloat16)
    qkv_grad = jnp.stack([query_grad, key_grad, value_grad], axis=2).reshape(JOINTS, FRAMES, 3 * hd)
    grad_scale = 1.0 / (JOINTS * FRAMES) ** 0.5
    frame_group = FRAMES // N_FRAME
    blocks_in = scaled.reshape(N_JOINT, group, N_FRAME, frame_group, D).transpose(0, 2, 1, 3, 4)
    blocks_in = blocks_in.reshape(N_JOINT * N_FRAME, group * frame_group, D)
    blocks_out = qkv_grad.reshape(N_JOINT, group, N_FRAME, frame_group, 3 * hd).transpose(0, 2, 1, 3, 4)
    blocks_out = blocks_out.reshape(N_JOINT * N_FRAME, group * frame_group, 3 * hd)

    def accumulate(total, pair):
        left, right = pair
        term = jnp.dot(left.T, right, preferred_element_type=jnp.float32) * grad_scale
        return (total + term.astype(jnp.bfloat16).astype(jnp.float32), None)
    weight_grad, unused = lax.scan(accumulate, jnp.zeros((D, 3 * hd), jnp.float32), (blocks_in, blocks_out))
    normed_grad = jnp.dot(qkv_grad.reshape(JOINTS * FRAMES, 3 * hd), qkv_weight.T, preferred_element_type=jnp.float32)
    normed_grad = normed_grad.reshape(JOINTS, FRAMES, D)
    gain_grad = lax.optimization_barrier(jnp.sum(normed_grad * normed, axis=(0, 1))) * grad_scale
    upper = normed_grad * gain32
    token_grad = (rinv * (upper - normed * lax.optimization_barrier(jnp.mean(upper * normed, axis=-1, keepdims=True)))).astype(jnp.bfloat16)
    return (attended, token_grad, weight_grad, gain_grad)
```

```python
import math

import jax
import jax.numpy as jnp
from jax import lax
from jax.sharding import PartitionSpec as P

HEADS = 8
HDIM = 128


EPSILON = 1e-05


def attention_local(queries, keys_all, values_all, upstream, inv_root, groups):
    scores = (
        jnp.einsum("fihd,fjhd->fhij", queries, keys_all, preferred_element_type=jnp.float32)
        * inv_root
    )
    probs = jax.nn.softmax(scores, axis=-1)
    probs_low = probs.astype(jnp.bfloat16)
    attended = jnp.einsum(
        "fhij,fjhd->fihd", probs_low, values_all, preferred_element_type=jnp.float32
    ).astype(jnp.bfloat16)
    prob_grad = jnp.einsum(
        "fihd,fjhd->fhij", upstream, values_all, preferred_element_type=jnp.float32
    )
    carried = jnp.sum(probs * prob_grad, axis=-1, keepdims=True)
    score_grad = (probs * (prob_grad - carried) * inv_root).astype(jnp.bfloat16)
    query_grad = jnp.einsum(
        "fhij,fjhd->fihd", score_grad, keys_all, preferred_element_type=jnp.float32
    ).astype(jnp.bfloat16)
    frames, joints = queries.shape[0], queries.shape[1]
    size = joints // groups
    sg = score_grad.reshape(frames, HEADS, groups, size, joints)
    pl_ = probs_low.reshape(frames, HEADS, groups, size, joints)
    qg = queries.reshape(frames, groups, size, HEADS, HDIM)
    ug = upstream.reshape(frames, groups, size, HEADS, HDIM)
    key_part = jnp.einsum("fhgij,fgihd->fgjhd", sg, qg, preferred_element_type=jnp.float32)
    value_part = jnp.einsum("fhgij,fgihd->fgjhd", pl_, ug, preferred_element_type=jnp.float32)
    key_grad = jnp.sum(key_part.astype(jnp.bfloat16).astype(jnp.float32), axis=1).astype(jnp.bfloat16)
    value_grad = jnp.sum(value_part.astype(jnp.bfloat16).astype(jnp.float32), axis=1).astype(
        jnp.bfloat16
    )
    return attended, query_grad, key_grad, value_grad


def per_device(tokens, norm_gain, qkv_weight, out_grad):
    joint_rows, frame_rows, width = tokens.shape
    inner = out_grad.shape[2]
    joint_count = lax.axis_size("joint")
    total_tokens = joint_rows * frame_rows * joint_count * lax.axis_size("frame")
    grad_scale = 1.0 / math.sqrt(total_tokens)
    inv_root = 1.0 / math.sqrt(HDIM)
    joints = joint_rows * joint_count
    local_frames = frame_rows // joint_count
    count = joints * local_frames

    whole = lax.all_gather(qkv_weight, "frame", axis=0, tiled=True)

    packed = jnp.concatenate([tokens, out_grad], axis=2)
    packed = lax.all_to_all(packed, "joint", 1, 0, tiled=True)
    packed = packed.transpose(1, 0, 2)
    flat = packed[:, :, :width].reshape(count, width).astype(jnp.float32)
    upstream = packed[:, :, width:].reshape(local_frames, joints, HEADS, HDIM)

    rinv = lax.rsqrt(jnp.mean(flat * flat, axis=1, keepdims=True) + EPSILON)
    normed = flat * rinv
    scaled = (normed * norm_gain).astype(jnp.bfloat16)
    projected = jnp.dot(scaled, whole, preferred_element_type=jnp.float32).astype(jnp.bfloat16)
    projected = projected.reshape(local_frames, joints, 3, HEADS, HDIM)
    queries = projected[:, :, 0]
    keys_all = projected[:, :, 1]
    values_all = projected[:, :, 2]
    attended, query_grad, key_grad, value_grad = attention_local(
        queries, keys_all, values_all, upstream, inv_root, joint_count
    )
    qkv_grad = jnp.concatenate(
        [
            query_grad.reshape(count, inner),
            key_grad.reshape(count, inner),
            value_grad.reshape(count, inner),
        ],
        axis=1,
    )
    product = lax.dot_general(
        scaled, qkv_grad, (((0,), (0,)), ((), ())), preferred_element_type=jnp.float32
    )
    frame_sum = lax.psum_scatter(
        (product * grad_scale).astype(jnp.bfloat16), "frame", scatter_dimension=0, tiled=True
    )
    joint_part = lax.psum_scatter(frame_sum, "joint", scatter_dimension=1, tiled=True)
    weight_grad = lax.all_gather(joint_part, "joint", axis=1, tiled=True).astype(jnp.float32)
    normed_grad = lax.dot_general(
        qkv_grad, whole, (((1,), (1,)), ((), ())), preferred_element_type=jnp.float32
    )
    gain_part = jnp.sum(normed_grad * normed, axis=0) * grad_scale
    gain_grad = lax.psum(gain_part, ("joint", "frame"))
    upper = normed_grad * norm_gain
    token_grad = rinv * (upper - normed * jnp.mean(upper * normed, axis=1, keepdims=True))
    token_grad = token_grad.astype(jnp.bfloat16).reshape(local_frames, joints, width)
    back = jnp.concatenate(
        [attended.reshape(local_frames, joints, inner), token_grad], axis=2
    ).transpose(1, 0, 2)
    back = lax.all_to_all(back, "joint", 0, 1, tiled=True)
    attended_out = back[:, :, :inner]
    token_out = back[:, :, inner:]
    return (attended_out, token_out, weight_grad, gain_grad)


def solution(mesh):
    placed = (P("joint", "frame", None), P(), P("frame", None), P("joint", "frame", None))
    return jax.shard_map(
        per_device,
        mesh=mesh,
        in_specs=placed,
        out_specs=(P("joint", "frame", None), P("joint", "frame", None), P("frame", None), P()),
        check_vma=False,
    )
```

```python
import math

import jax
import jax.numpy as jnp
from jax import lax
from jax.sharding import PartitionSpec as P

HEADS = 8
HDIM = 128


EPSILON = 1e-05


def attention_local(queries, keys_all, values_all, upstream, inv_root, groups):
    scores = (
        jnp.einsum("fihd,fjhd->fhij", queries, keys_all, preferred_element_type=jnp.float32)
        * inv_root
    )
    probs = jax.nn.softmax(scores, axis=-1)
    probs_low = probs.astype(jnp.bfloat16)
    attended = jnp.einsum(
        "fhij,fjhd->fihd", probs_low, values_all, preferred_element_type=jnp.float32
    ).astype(jnp.bfloat16)
    prob_grad = jnp.einsum(
        "fihd,fjhd->fhij", upstream, values_all, preferred_element_type=jnp.float32
    )
    carried = jnp.sum(probs * prob_grad, axis=-1, keepdims=True)
    score_grad = (probs * (prob_grad - carried) * inv_root).astype(jnp.bfloat16)
    query_grad = jnp.einsum(
        "fhij,fjhd->fihd", score_grad, keys_all, preferred_element_type=jnp.float32
    ).astype(jnp.bfloat16)
    frames, joints = queries.shape[0], queries.shape[1]
    size = joints // groups
    sg = score_grad.reshape(frames, HEADS, groups, size, joints)
    pl_ = probs_low.reshape(frames, HEADS, groups, size, joints)
    qg = queries.reshape(frames, groups, size, HEADS, HDIM)
    ug = upstream.reshape(frames, groups, size, HEADS, HDIM)
    key_part = jnp.einsum("fhgij,fgihd->fgjhd", sg, qg, preferred_element_type=jnp.float32)
    value_part = jnp.einsum("fhgij,fgihd->fgjhd", pl_, ug, preferred_element_type=jnp.float32)
    key_grad = jnp.sum(key_part.astype(jnp.bfloat16).astype(jnp.float32), axis=1).astype(jnp.bfloat16)
    value_grad = jnp.sum(value_part.astype(jnp.bfloat16).astype(jnp.float32), axis=1).astype(
        jnp.bfloat16
    )
    return attended, query_grad, key_grad, value_grad


def per_device(tokens, norm_gain, qkv_weight, out_grad):
    joint_rows, frame_rows, width = tokens.shape
    inner = out_grad.shape[2]
    joint_count = lax.axis_size("joint")
    total_tokens = joint_rows * frame_rows * joint_count * lax.axis_size("frame")
    grad_scale = 1.0 / math.sqrt(total_tokens)
    inv_root = 1.0 / math.sqrt(HDIM)
    joints = joint_rows * joint_count
    local_frames = frame_rows // joint_count
    count = joints * local_frames

    whole = lax.all_gather(qkv_weight, "frame", axis=0, tiled=True)

    packed = jnp.concatenate([tokens, out_grad], axis=2)
    packed = lax.all_to_all(packed, "joint", 1, 0, tiled=True)
    packed = packed.transpose(1, 0, 2)
    flat = packed[:, :, :width].reshape(count, width).astype(jnp.float32)
    upstream = packed[:, :, width:].reshape(local_frames, joints, HEADS, HDIM)

    rinv = lax.rsqrt(jnp.mean(flat * flat, axis=1, keepdims=True) + EPSILON)
    normed = flat * rinv
    scaled = (normed * norm_gain).astype(jnp.bfloat16)
    projected = jnp.dot(scaled, whole, preferred_element_type=jnp.float32).astype(jnp.bfloat16)
    projected = projected.reshape(local_frames, joints, 3, HEADS, HDIM)
    queries = projected[:, :, 0]
    keys_all = projected[:, :, 1]
    values_all = projected[:, :, 2]
    attended, query_grad, key_grad, value_grad = attention_local(
        queries, keys_all, values_all, upstream, inv_root, joint_count
    )
    qkv_grad = jnp.concatenate(
        [
            query_grad.reshape(count, inner),
            key_grad.reshape(count, inner),
            value_grad.reshape(count, inner),
        ],
        axis=1,
    )
    frame_count = lax.axis_size("frame")
    col_block = 3 * inner // joint_count
    product = jnp.einsum(
        "tk,tjc->jkc",
        scaled,
        qkv_grad.reshape(count, joint_count, col_block),
        preferred_element_type=jnp.float32,
    )
    product = (product * grad_scale).astype(jnp.bfloat16)
    product = product.reshape(joint_count * frame_count, width // frame_count, col_block)
    block = lax.psum_scatter(product, ("joint", "frame"), scatter_dimension=0, tiled=True)
    weight_grad = lax.all_gather(block, "joint", axis=0, tiled=True)
    weight_grad = weight_grad.transpose(1, 0, 2).reshape(width // frame_count, 3 * inner)
    weight_grad = weight_grad.astype(jnp.float32)
    normed_grad = lax.dot_general(
        qkv_grad, whole, (((1,), (1,)), ((), ())), preferred_element_type=jnp.float32
    )
    gain_part = jnp.sum(normed_grad * normed, axis=0) * grad_scale
    gain_grad = lax.psum(lax.psum(gain_part, "frame"), "joint")
    upper = normed_grad * norm_gain
    token_grad = rinv * (upper - normed * jnp.mean(upper * normed, axis=1, keepdims=True))
    token_grad = token_grad.astype(jnp.bfloat16).reshape(local_frames, joints, width)
    back = jnp.concatenate(
        [attended.reshape(local_frames, joints, inner), token_grad], axis=2
    ).transpose(1, 0, 2)
    back = lax.all_to_all(back, "joint", 0, 1, tiled=True)
    attended_out = back[:, :, :inner]
    token_out = back[:, :, inner:]
    return (attended_out, token_out, weight_grad, gain_grad)


def solution(mesh):
    placed = (P("joint", "frame", None), P(), P("frame", None), P("joint", "frame", None))
    return jax.shard_map(
        per_device,
        mesh=mesh,
        in_specs=placed,
        out_specs=(P("joint", "frame", None), P("joint", "frame", None), P("frame", None), P()),
        check_vma=False,
    )
```

```python
import math

import jax
import jax.numpy as jnp
from jax import lax
from jax.sharding import PartitionSpec as P

HEADS = 8
HDIM = 128


EPSILON = 1e-05


def attention_local(queries, keys_all, values_all, upstream, inv_root, groups):
    scores = (
        jnp.einsum("fihd,fjhd->fhij", queries, keys_all, preferred_element_type=jnp.float32)
        * inv_root
    )
    probs = jax.nn.softmax(scores, axis=-1)
    probs_low = probs.astype(jnp.bfloat16)
    attended = jnp.einsum(
        "fhij,fjhd->fihd", probs_low, values_all, preferred_element_type=jnp.float32
    ).astype(jnp.bfloat16)
    prob_grad = jnp.einsum(
        "fihd,fjhd->fhij", upstream, values_all, preferred_element_type=jnp.float32
    )
    carried = jnp.sum(probs * prob_grad, axis=-1, keepdims=True)
    score_grad = (probs * (prob_grad - carried) * inv_root).astype(jnp.bfloat16)
    query_grad = jnp.einsum(
        "fhij,fjhd->fihd", score_grad, keys_all, preferred_element_type=jnp.float32
    ).astype(jnp.bfloat16)
    frames, joints = queries.shape[0], queries.shape[1]
    size = joints // groups
    sg = score_grad.reshape(frames, HEADS, groups, size, joints)
    pl_ = probs_low.reshape(frames, HEADS, groups, size, joints)
    qg = queries.reshape(frames, groups, size, HEADS, HDIM)
    ug = upstream.reshape(frames, groups, size, HEADS, HDIM)
    key_part = jnp.einsum("fhgij,fgihd->fgjhd", sg, qg, preferred_element_type=jnp.float32)
    value_part = jnp.einsum("fhgij,fgihd->fgjhd", pl_, ug, preferred_element_type=jnp.float32)
    key_grad = jnp.sum(key_part.astype(jnp.bfloat16).astype(jnp.float32), axis=1).astype(jnp.bfloat16)
    value_grad = jnp.sum(value_part.astype(jnp.bfloat16).astype(jnp.float32), axis=1).astype(
        jnp.bfloat16
    )
    return attended, query_grad, key_grad, value_grad


def per_device(tokens, norm_gain, qkv_weight, out_grad):
    joint_rows, frame_rows, width = tokens.shape
    inner = out_grad.shape[2]
    joint_count = lax.axis_size("joint")
    chips = lax.axis_size("chip")
    cores = lax.axis_size("core")
    total_tokens = joint_rows * frame_rows * joint_count * chips * cores
    grad_scale = 1.0 / math.sqrt(total_tokens)
    inv_root = 1.0 / math.sqrt(HDIM)
    joints = joint_rows * joint_count
    local_frames = frame_rows // joint_count
    count = joints * local_frames

    whole = lax.all_gather(qkv_weight, "chip", axis=0, tiled=True)
    whole = lax.all_gather(whole, "core", axis=0, tiled=True)
    rows = width // (chips * cores)

    def to_fine(x):
        lead = x.shape[:-1]
        x = x.reshape(lead + (chips, cores, rows))
        return jnp.swapaxes(x, -3, -2).reshape(lead + (width,))

    def from_fine(x):
        lead = x.shape[:-1]
        x = x.reshape(lead + (cores, chips, rows))
        return jnp.swapaxes(x, -3, -2).reshape(lead + (width,))

    gain_fine = to_fine(norm_gain)

    packed = jnp.concatenate([tokens, out_grad], axis=2)
    packed = lax.all_to_all(packed, "joint", 1, 0, tiled=True)
    packed = packed.transpose(1, 0, 2)
    flat = to_fine(packed[:, :, :width].reshape(count, width)).astype(jnp.float32)
    upstream = packed[:, :, width:].reshape(local_frames, joints, HEADS, HDIM)

    rinv = lax.rsqrt(jnp.mean(flat * flat, axis=1, keepdims=True) + EPSILON)
    normed = flat * rinv
    scaled = (normed * gain_fine).astype(jnp.bfloat16)
    projected = jnp.dot(scaled, whole, preferred_element_type=jnp.float32).astype(jnp.bfloat16)
    projected = projected.reshape(local_frames, joints, 3, HEADS, HDIM)
    queries = projected[:, :, 0]
    keys_all = projected[:, :, 1]
    values_all = projected[:, :, 2]
    attended, query_grad, key_grad, value_grad = attention_local(
        queries, keys_all, values_all, upstream, inv_root, joint_count
    )
    qkv_grad = jnp.concatenate(
        [
            query_grad.reshape(count, inner),
            key_grad.reshape(count, inner),
            value_grad.reshape(count, inner),
        ],
        axis=1,
    )
    product = lax.dot_general(
        scaled, qkv_grad, (((0,), (0,)), ((), ())), preferred_element_type=jnp.float32
    )
    part = (product * grad_scale).astype(jnp.bfloat16)
    part = lax.psum_scatter(part, "core", scatter_dimension=0, tiled=True)
    frame_sum = lax.psum_scatter(part, "chip", scatter_dimension=0, tiled=True)
    joint_part = lax.psum_scatter(frame_sum, "joint", scatter_dimension=1, tiled=True)
    weight_grad = lax.all_gather(joint_part, "joint", axis=1, tiled=True).astype(jnp.float32)
    normed_grad = lax.dot_general(
        qkv_grad, whole, (((1,), (1,)), ((), ())), preferred_element_type=jnp.float32
    )
    gain_part = jnp.sum(normed_grad * normed, axis=0) * grad_scale
    gain_grad = from_fine(lax.psum(gain_part, ("joint", "chip", "core")))
    upper = normed_grad * gain_fine
    token_grad = rinv * (upper - normed * jnp.mean(upper * normed, axis=1, keepdims=True))
    token_grad = from_fine(token_grad.astype(jnp.bfloat16)).reshape(local_frames, joints, width)
    back = jnp.concatenate(
        [attended.reshape(local_frames, joints, inner), token_grad], axis=2
    ).transpose(1, 0, 2)
    back = lax.all_to_all(back, "joint", 0, 1, tiled=True)
    attended_out = back[:, :, :inner]
    token_out = back[:, :, inner:]
    return (attended_out, token_out, weight_grad, gain_grad)


def solution(mesh):
    joint_count, frame_count = mesh.devices.shape
    fine = jax.sharding.Mesh(
        mesh.devices.reshape(joint_count, frame_count // 2, 2), ("joint", "chip", "core")
    )
    frame = ("chip", "core")
    placed = (P("joint", frame, None), P(), P(frame, None), P("joint", frame, None))
    return jax.shard_map(
        per_device,
        mesh=fine,
        in_specs=placed,
        out_specs=(P("joint", frame, None), P("joint", frame, None), P(frame, None), P()),
        check_vma=False,
    )
```

```python
import math

import jax
import jax.numpy as jnp
from jax import lax
from jax.sharding import PartitionSpec as P


HEADS = 8
HDIM = 128


EPSILON = 1e-05
SIDE_COLS = 768


def attention_local(queries, keys_all, values_all, upstream, inv_root, groups):
    scores = (
        jnp.einsum("fihd,fjhd->fhij", queries, keys_all, preferred_element_type=jnp.float32)
        * inv_root
    )
    probs = jax.nn.softmax(scores, axis=-1)
    probs_low = probs.astype(jnp.bfloat16)
    attended = jnp.einsum(
        "fhij,fjhd->fihd", probs_low, values_all, preferred_element_type=jnp.float32
    ).astype(jnp.bfloat16)
    prob_grad = jnp.einsum(
        "fihd,fjhd->fhij", upstream, values_all, preferred_element_type=jnp.float32
    )
    carried = jnp.sum(probs * prob_grad, axis=-1, keepdims=True)
    score_grad = (probs * (prob_grad - carried) * inv_root).astype(jnp.bfloat16)
    query_grad = jnp.einsum(
        "fhij,fjhd->fihd", score_grad, keys_all, preferred_element_type=jnp.float32
    ).astype(jnp.bfloat16)
    frames, joints = queries.shape[0], queries.shape[1]
    size = joints // groups
    sg = score_grad.reshape(frames, HEADS, groups, size, joints)
    pl_ = probs_low.reshape(frames, HEADS, groups, size, joints)
    qg = queries.reshape(frames, groups, size, HEADS, HDIM)
    ug = upstream.reshape(frames, groups, size, HEADS, HDIM)
    key_part = jnp.einsum("fhgij,fgihd->fgjhd", sg, qg, preferred_element_type=jnp.float32)
    value_part = jnp.einsum("fhgij,fgihd->fgjhd", pl_, ug, preferred_element_type=jnp.float32)
    key_grad = jnp.sum(key_part.astype(jnp.bfloat16).astype(jnp.float32), axis=1).astype(jnp.bfloat16)
    value_grad = jnp.sum(value_part.astype(jnp.bfloat16).astype(jnp.float32), axis=1).astype(
        jnp.bfloat16
    )
    return attended, query_grad, key_grad, value_grad


def per_device_body(tokens, norm_gain, qkv_weight, out_grad):
    joint_rows, frame_rows, width = tokens.shape
    inner = out_grad.shape[2]
    joint_count = lax.axis_size("joint")
    total_tokens = joint_rows * frame_rows * joint_count * lax.axis_size("frame")
    grad_scale = 1.0 / math.sqrt(total_tokens)
    inv_root = 1.0 / math.sqrt(HDIM)
    joints = joint_rows * joint_count
    local_frames = frame_rows // joint_count
    count = joints * local_frames

    whole = lax.all_gather(qkv_weight, "frame", axis=0, tiled=True)

    packed = jnp.concatenate([tokens, out_grad], axis=2)
    packed = lax.all_to_all(packed, "joint", 1, 0, tiled=True)
    packed = packed.transpose(1, 0, 2)
    flat = packed[:, :, :width].reshape(count, width).astype(jnp.float32)
    upstream = packed[:, :, width:].reshape(local_frames, joints, HEADS, HDIM)

    rinv = lax.rsqrt(jnp.mean(flat * flat, axis=1, keepdims=True) + EPSILON)
    normed = flat * rinv
    scaled = (normed * norm_gain).astype(jnp.bfloat16)
    projected = jnp.dot(scaled, whole, preferred_element_type=jnp.float32).astype(jnp.bfloat16)
    projected = projected.reshape(local_frames, joints, 3, HEADS, HDIM)
    queries = projected[:, :, 0]
    keys_all = projected[:, :, 1]
    values_all = projected[:, :, 2]
    attended, query_grad, key_grad, value_grad = attention_local(
        queries, keys_all, values_all, upstream, inv_root, joint_count
    )
    qkv_grad = jnp.concatenate(
        [
            query_grad.reshape(count, inner),
            key_grad.reshape(count, inner),
            value_grad.reshape(count, inner),
        ],
        axis=1,
    )
    product = lax.dot_general(
        scaled, qkv_grad, (((0,), (0,)), ((), ())), preferred_element_type=jnp.float32
    )
    frame_count = lax.axis_size("frame")
    row_count = width // frame_count
    col_block = 3 * inner // joint_count
    ring_cols = 3 * inner - SIDE_COLS
    part = (product * grad_scale).astype(jnp.bfloat16)
    ring_sum = lax.psum_scatter(part[:, :ring_cols], "frame", scatter_dimension=0, tiled=True)
    normed_grad = lax.dot_general(
        qkv_grad, whole, (((1,), (1,)), ((), ())), preferred_element_type=jnp.float32
    )
    gain_part = (jnp.sum(normed_grad * normed, axis=0) * grad_scale).reshape(row_count, width // row_count)
    gain_high = gain_part.astype(jnp.bfloat16)
    gain_low = (gain_part - gain_high.astype(jnp.float32)).astype(jnp.bfloat16)
    side = jnp.concatenate(
        [
            part[:, ring_cols:].reshape(frame_count, row_count, SIDE_COLS),
            jnp.broadcast_to(gain_high[None], (frame_count,) + gain_high.shape),
            jnp.broadcast_to(gain_low[None], (frame_count,) + gain_low.shape),
        ],
        axis=2,
    )
    side = lax.all_to_all(side, "frame", 0, 0, tiled=True)
    side = jnp.sum(side.astype(jnp.float32), axis=0)
    gain_cols = width // row_count
    side_sum = side[:, :SIDE_COLS]
    gain_sum = side[:, SIDE_COLS:SIDE_COLS + gain_cols] + side[:, SIDE_COLS + gain_cols:]
    frame_sum = jnp.concatenate([ring_sum.astype(jnp.float32), side_sum], axis=1)
    blocks = frame_sum.reshape(row_count, joint_count, col_block).transpose(1, 0, 2)
    first = (lax.broadcasted_iota(jnp.int32, (joint_count, 1, 1), 0) == 0).astype(jnp.float32)
    blocks = jnp.concatenate([blocks, first * gain_sum[None]], axis=2)
    blocks = lax.all_to_all(blocks, "joint", 0, 0, tiled=True)
    block_sum = jnp.sum(blocks, axis=0)
    spread = jnp.broadcast_to(block_sum[None], (joint_count,) + block_sum.shape)
    spread = lax.all_to_all(spread, "joint", 0, 0, tiled=True)
    weight_grad = spread[:, :, :col_block].transpose(1, 0, 2).reshape(row_count, 3 * inner)
    gain_grad = spread[0, :, col_block:].reshape(width)
    upper = normed_grad * norm_gain
    token_grad = rinv * (upper - normed * jnp.mean(upper * normed, axis=1, keepdims=True))
    token_grad = token_grad.astype(jnp.bfloat16).reshape(local_frames, joints, width)
    back = jnp.concatenate(
        [attended.reshape(local_frames, joints, inner), token_grad], axis=2
    ).transpose(1, 0, 2)
    back = lax.all_to_all(back, "joint", 0, 1, tiled=True)
    attended_out = back[:, :, :inner]
    token_out = back[:, :, inner:]
    return (attended_out, token_out, weight_grad, gain_grad)


def solution(mesh):
    placed = (P("joint", "frame", None), P(), P("frame", None), P("joint", "frame", None))
    return jax.shard_map(
        per_device_body,
        mesh=mesh,
        in_specs=placed,
        out_specs=(P("joint", "frame", None), P("joint", "frame", None), P("frame", None), P()),
        check_vma=False,
    )
```

```python
import math

import jax
import jax.numpy as jnp
from jax import lax
from jax.sharding import PartitionSpec as P


HEADS = 8
HDIM = 128


EPSILON = 1e-05


def attention_local(queries, keys_all, values_all, upstream, inv_root, groups):
    scores = (
        jnp.einsum("fihd,fjhd->fhij", queries, keys_all, preferred_element_type=jnp.float32)
        * inv_root
    )
    probs = jax.nn.softmax(scores, axis=-1)
    probs_low = probs.astype(jnp.bfloat16)
    attended = jnp.einsum(
        "fhij,fjhd->fihd", probs_low, values_all, preferred_element_type=jnp.float32
    ).astype(jnp.bfloat16)
    prob_grad = jnp.einsum(
        "fihd,fjhd->fhij", upstream, values_all, preferred_element_type=jnp.float32
    )
    carried = jnp.sum(probs * prob_grad, axis=-1, keepdims=True)
    score_grad = (probs * (prob_grad - carried) * inv_root).astype(jnp.bfloat16)
    query_grad = jnp.einsum(
        "fhij,fjhd->fihd", score_grad, keys_all, preferred_element_type=jnp.float32
    ).astype(jnp.bfloat16)
    frames, joints = queries.shape[0], queries.shape[1]
    size = joints // groups
    sg = score_grad.reshape(frames, HEADS, groups, size, joints)
    pl_ = probs_low.reshape(frames, HEADS, groups, size, joints)
    qg = queries.reshape(frames, groups, size, HEADS, HDIM)
    ug = upstream.reshape(frames, groups, size, HEADS, HDIM)
    key_part = jnp.einsum("fhgij,fgihd->fgjhd", sg, qg, preferred_element_type=jnp.float32)
    value_part = jnp.einsum("fhgij,fgihd->fgjhd", pl_, ug, preferred_element_type=jnp.float32)
    key_grad = jnp.sum(key_part.astype(jnp.bfloat16).astype(jnp.float32), axis=1).astype(jnp.bfloat16)
    value_grad = jnp.sum(value_part.astype(jnp.bfloat16).astype(jnp.float32), axis=1).astype(
        jnp.bfloat16
    )
    return attended, query_grad, key_grad, value_grad


def per_device_body(tokens, norm_gain, qkv_weight, out_grad):
    joint_rows, frame_rows, width = tokens.shape
    inner = out_grad.shape[2]
    joint_count = lax.axis_size("joint")
    total_tokens = joint_rows * frame_rows * joint_count * lax.axis_size("frame")
    grad_scale = 1.0 / math.sqrt(total_tokens)
    inv_root = 1.0 / math.sqrt(HDIM)
    joints = joint_rows * joint_count
    local_frames = frame_rows // joint_count
    count = joints * local_frames

    whole = lax.all_gather(qkv_weight, "frame", axis=0, tiled=True)

    packed = jnp.concatenate([tokens, out_grad], axis=2)
    packed = lax.all_to_all(packed, "joint", 1, 0, tiled=True)
    packed = packed.transpose(1, 0, 2)
    flat = packed[:, :, :width].reshape(count, width).astype(jnp.float32)
    upstream = packed[:, :, width:].reshape(local_frames, joints, HEADS, HDIM)

    rinv = lax.rsqrt(jnp.mean(flat * flat, axis=1, keepdims=True) + EPSILON)
    normed = flat * rinv
    scaled = (normed * norm_gain).astype(jnp.bfloat16)
    projected = jnp.dot(scaled, whole, preferred_element_type=jnp.float32).astype(jnp.bfloat16)
    projected = projected.reshape(local_frames, joints, 3, HEADS, HDIM)
    queries = projected[:, :, 0]
    keys_all = projected[:, :, 1]
    values_all = projected[:, :, 2]
    attended, query_grad, key_grad, value_grad = attention_local(
        queries, keys_all, values_all, upstream, inv_root, joint_count
    )
    qkv_grad = jnp.concatenate(
        [
            query_grad.reshape(count, inner),
            key_grad.reshape(count, inner),
            value_grad.reshape(count, inner),
        ],
        axis=1,
    )
    product = lax.dot_general(
        scaled, qkv_grad, (((0,), (0,)), ((), ())), preferred_element_type=jnp.float32
    )
    frame_sum = lax.psum_scatter(
        (product * grad_scale).astype(jnp.bfloat16), "frame", scatter_dimension=0, tiled=True
    )
    row_count = frame_sum.shape[0]
    col_block = 3 * inner // joint_count
    blocks = frame_sum.reshape(row_count, joint_count, col_block).transpose(1, 0, 2)
    blocks = lax.all_to_all(blocks, "joint", 0, 0, tiled=True)
    block_sum = jnp.sum(blocks.astype(jnp.float32), axis=0)
    spread = jnp.broadcast_to(block_sum.astype(jnp.bfloat16)[None], (joint_count, row_count, col_block))
    spread = lax.all_to_all(spread, "joint", 0, 0, tiled=True)
    weight_grad = spread.transpose(1, 0, 2).reshape(row_count, 3 * inner).astype(jnp.float32)
    normed_grad = lax.dot_general(
        qkv_grad, whole, (((1,), (1,)), ((), ())), preferred_element_type=jnp.float32
    )
    gain_part = jnp.sum(normed_grad * normed, axis=0) * grad_scale
    gain_grad = lax.psum(gain_part, ("joint", "frame"))
    upper = normed_grad * norm_gain
    token_grad = rinv * (upper - normed * jnp.mean(upper * normed, axis=1, keepdims=True))
    token_grad = token_grad.astype(jnp.bfloat16).reshape(local_frames, joints, width)
    back = jnp.concatenate(
        [attended.reshape(local_frames, joints, inner), token_grad], axis=2
    ).transpose(1, 0, 2)
    back = lax.all_to_all(back, "joint", 0, 1, tiled=True)
    attended_out = back[:, :, :inner]
    token_out = back[:, :, inner:]
    return (attended_out, token_out, weight_grad, gain_grad)


def solution(mesh):
    placed = (P("joint", "frame", None), P(), P("frame", None), P("joint", "frame", None))
    return jax.shard_map(
        per_device_body,
        mesh=mesh,
        in_specs=placed,
        out_specs=(P("joint", "frame", None), P("joint", "frame", None), P("frame", None), P()),
        check_vma=False,
    )
```

```python
import math

import jax
import jax.numpy as jnp
from jax import lax
from jax.sharding import PartitionSpec as P


HEADS = 8
HDIM = 128


EPSILON = 1e-05


def attention_local(queries, keys_all, values_all, upstream, inv_root, groups):
    scores = (
        jnp.einsum("fihd,fjhd->fhij", queries, keys_all, preferred_element_type=jnp.float32)
        * inv_root
    )
    probs = jax.nn.softmax(scores, axis=-1)
    probs_low = probs.astype(jnp.bfloat16)
    attended = jnp.einsum(
        "fhij,fjhd->fihd", probs_low, values_all, preferred_element_type=jnp.float32
    ).astype(jnp.bfloat16)
    prob_grad = jnp.einsum(
        "fihd,fjhd->fhij", upstream, values_all, preferred_element_type=jnp.float32
    )
    carried = jnp.sum(probs * prob_grad, axis=-1, keepdims=True)
    score_grad = (probs * (prob_grad - carried) * inv_root).astype(jnp.bfloat16)
    query_grad = jnp.einsum(
        "fhij,fjhd->fihd", score_grad, keys_all, preferred_element_type=jnp.float32
    ).astype(jnp.bfloat16)
    frames, joints = queries.shape[0], queries.shape[1]
    size = joints // groups
    sg = score_grad.reshape(frames, HEADS, groups, size, joints)
    pl_ = probs_low.reshape(frames, HEADS, groups, size, joints)
    qg = queries.reshape(frames, groups, size, HEADS, HDIM)
    ug = upstream.reshape(frames, groups, size, HEADS, HDIM)
    key_part = jnp.einsum("fhgij,fgihd->fgjhd", sg, qg, preferred_element_type=jnp.float32)
    value_part = jnp.einsum("fhgij,fgihd->fgjhd", pl_, ug, preferred_element_type=jnp.float32)
    key_grad = jnp.sum(key_part.astype(jnp.bfloat16).astype(jnp.float32), axis=1).astype(jnp.bfloat16)
    value_grad = jnp.sum(value_part.astype(jnp.bfloat16).astype(jnp.float32), axis=1).astype(
        jnp.bfloat16
    )
    return attended, query_grad, key_grad, value_grad


def per_device_body(tokens, norm_gain, qkv_weight, out_grad):
    joint_rows, frame_rows, width = tokens.shape
    inner = out_grad.shape[2]
    joint_count = lax.axis_size("joint")
    total_tokens = joint_rows * frame_rows * joint_count * lax.axis_size("frame")
    grad_scale = 1.0 / math.sqrt(total_tokens)
    inv_root = 1.0 / math.sqrt(HDIM)
    joints = joint_rows * joint_count
    local_frames = frame_rows // joint_count
    count = joints * local_frames

    whole = lax.all_gather(qkv_weight, "frame", axis=0, tiled=True)

    packed = jnp.concatenate([tokens, out_grad], axis=2)
    packed = lax.all_to_all(packed, "joint", 1, 0, tiled=True)
    packed = packed.transpose(1, 0, 2)
    flat = packed[:, :, :width].reshape(count, width).astype(jnp.float32)
    upstream = packed[:, :, width:].reshape(local_frames, joints, HEADS, HDIM)

    rinv = lax.rsqrt(jnp.mean(flat * flat, axis=1, keepdims=True) + EPSILON)
    normed = flat * rinv
    scaled = (normed * norm_gain).astype(jnp.bfloat16)
    projected = jnp.dot(scaled, whole, preferred_element_type=jnp.float32).astype(jnp.bfloat16)
    projected = projected.reshape(local_frames, joints, 3, HEADS, HDIM)
    queries = projected[:, :, 0]
    keys_all = projected[:, :, 1]
    values_all = projected[:, :, 2]
    attended, query_grad, key_grad, value_grad = attention_local(
        queries, keys_all, values_all, upstream, inv_root, joint_count
    )
    qkv_grad = jnp.concatenate(
        [
            query_grad.reshape(count, inner),
            key_grad.reshape(count, inner),
            value_grad.reshape(count, inner),
        ],
        axis=1,
    )
    value_product = lax.dot_general(
        scaled, value_grad.reshape(count, inner), (((0,), (0,)), ((), ())),
        preferred_element_type=jnp.float32,
    )
    value_sum = lax.psum_scatter(
        (value_product * grad_scale).astype(jnp.bfloat16), "frame", scatter_dimension=0, tiled=True
    )
    product = lax.dot_general(
        scaled, qkv_grad[:, : 2 * inner], (((0,), (0,)), ((), ())), preferred_element_type=jnp.float32
    )
    frame_sum = lax.psum_scatter((product * grad_scale).astype(jnp.bfloat16), "frame", scatter_dimension=0, tiled=True)
    frame_sum = jnp.concatenate([frame_sum, value_sum], axis=1)
    row_count = frame_sum.shape[0]
    col_block = 3 * inner // joint_count
    blocks = frame_sum.reshape(row_count, joint_count, col_block).transpose(1, 0, 2)
    blocks = lax.all_to_all(blocks, "joint", 0, 0, tiled=True)
    block_sum = jnp.sum(blocks.astype(jnp.float32), axis=0)
    spread = jnp.broadcast_to(block_sum.astype(jnp.bfloat16)[None], (joint_count, row_count, col_block))
    spread = lax.all_to_all(spread, "joint", 0, 0, tiled=True)
    weight_grad = spread.transpose(1, 0, 2).reshape(row_count, 3 * inner).astype(jnp.float32)
    normed_grad = lax.dot_general(
        qkv_grad, whole, (((1,), (1,)), ((), ())), preferred_element_type=jnp.float32
    )
    gain_part = jnp.sum(normed_grad * normed, axis=0) * grad_scale
    gain_grad = lax.psum(gain_part, ("joint", "frame"))
    upper = normed_grad * norm_gain
    token_grad = rinv * (upper - normed * jnp.mean(upper * normed, axis=1, keepdims=True))
    token_grad = token_grad.astype(jnp.bfloat16).reshape(local_frames, joints, width)
    back = jnp.concatenate(
        [attended.reshape(local_frames, joints, inner), token_grad], axis=2
    ).transpose(1, 0, 2)
    back = lax.all_to_all(back, "joint", 0, 1, tiled=True)
    attended_out = back[:, :, :inner]
    token_out = back[:, :, inner:]
    return (attended_out, token_out, weight_grad, gain_grad)


def solution(mesh):
    placed = (P("joint", "frame", None), P(), P("frame", None), P("joint", "frame", None))
    return jax.shard_map(
        per_device_body,
        mesh=mesh,
        in_specs=placed,
        out_specs=(P("joint", "frame", None), P("joint", "frame", None), P("frame", None), P()),
        check_vma=False,
    )
```

```python
import math

import jax
import jax.numpy as jnp
from jax import lax
from jax.sharding import PartitionSpec as P


HEADS = 8
HDIM = 128


EPSILON = 1e-05


def attention_local(queries, keys_all, values_all, upstream, inv_root, groups):
    scores = (
        jnp.einsum("fihd,fjhd->fhij", queries, keys_all, preferred_element_type=jnp.float32)
        * inv_root
    )
    probs = jax.nn.softmax(scores, axis=-1)
    probs_low = probs.astype(jnp.bfloat16)
    attended = jnp.einsum(
        "fhij,fjhd->fihd", probs_low, values_all, preferred_element_type=jnp.float32
    ).astype(jnp.bfloat16)
    prob_grad = jnp.einsum(
        "fihd,fjhd->fhij", upstream, values_all, preferred_element_type=jnp.float32
    )
    carried = jnp.sum(probs * prob_grad, axis=-1, keepdims=True)
    score_grad = (probs * (prob_grad - carried) * inv_root).astype(jnp.bfloat16)
    query_grad = jnp.einsum(
        "fhij,fjhd->fihd", score_grad, keys_all, preferred_element_type=jnp.float32
    ).astype(jnp.bfloat16)
    frames, joints = queries.shape[0], queries.shape[1]
    size = joints // groups
    sg = score_grad.reshape(frames, HEADS, groups, size, joints)
    pl_ = probs_low.reshape(frames, HEADS, groups, size, joints)
    qg = queries.reshape(frames, groups, size, HEADS, HDIM)
    ug = upstream.reshape(frames, groups, size, HEADS, HDIM)
    key_part = jnp.einsum("fhgij,fgihd->fgjhd", sg, qg, preferred_element_type=jnp.float32)
    value_part = jnp.einsum("fhgij,fgihd->fgjhd", pl_, ug, preferred_element_type=jnp.float32)
    key_grad = jnp.sum(key_part.astype(jnp.bfloat16).astype(jnp.float32), axis=1).astype(jnp.bfloat16)
    value_grad = jnp.sum(value_part.astype(jnp.bfloat16).astype(jnp.float32), axis=1).astype(
        jnp.bfloat16
    )
    return attended, query_grad, key_grad, value_grad


def per_device_body(tokens, norm_gain, qkv_weight, out_grad):
    joint_rows, frame_rows, width = tokens.shape
    inner = out_grad.shape[2]
    joint_count = lax.axis_size("joint")
    total_tokens = joint_rows * frame_rows * joint_count * lax.axis_size("frame")
    grad_scale = 1.0 / math.sqrt(total_tokens)
    inv_root = 1.0 / math.sqrt(HDIM)
    joints = joint_rows * joint_count
    local_frames = frame_rows // joint_count
    count = joints * local_frames

    whole = lax.all_gather(qkv_weight, "frame", axis=0, tiled=True)

    packed = jnp.concatenate([tokens, out_grad], axis=2)
    packed = lax.all_to_all(packed, "joint", 1, 0, tiled=True)
    packed = packed.transpose(1, 0, 2)
    flat = packed[:, :, :width].reshape(count, width).astype(jnp.float32)
    upstream = packed[:, :, width:].reshape(local_frames, joints, HEADS, HDIM)

    rinv = lax.rsqrt(jnp.mean(flat * flat, axis=1, keepdims=True) + EPSILON)
    normed = flat * rinv
    scaled = (normed * norm_gain).astype(jnp.bfloat16)
    projected = jnp.dot(scaled, whole, preferred_element_type=jnp.float32).astype(jnp.bfloat16)
    projected = projected.reshape(local_frames, joints, 3, HEADS, HDIM)
    queries = projected[:, :, 0]
    keys_all = projected[:, :, 1]
    values_all = projected[:, :, 2]
    attended, query_grad, key_grad, value_grad = attention_local(
        queries, keys_all, values_all, upstream, inv_root, joint_count
    )
    qkv_grad = jnp.concatenate(
        [
            query_grad.reshape(count, inner),
            key_grad.reshape(count, inner),
            value_grad.reshape(count, inner),
        ],
        axis=1,
    )
    product = lax.dot_general(
        scaled, qkv_grad, (((0,), (0,)), ((), ())), preferred_element_type=jnp.float32
    )
    frame_sum = lax.psum_scatter(
        (product * grad_scale).astype(jnp.bfloat16), "frame", scatter_dimension=0, tiled=True
    )
    weight_grad = frame_sum
    step = 1
    while step < joint_count:
        pairs = [(j, j ^ step) for j in range(joint_count)]
        other = lax.ppermute(weight_grad, "joint", pairs)
        weight_grad = (weight_grad.astype(jnp.float32) + other.astype(jnp.float32)).astype(jnp.bfloat16)
        step *= 2
    weight_grad = weight_grad.astype(jnp.float32)
    normed_grad = lax.dot_general(
        qkv_grad, whole, (((1,), (1,)), ((), ())), preferred_element_type=jnp.float32
    )
    gain_part = jnp.sum(normed_grad * normed, axis=0) * grad_scale
    gain_grad = lax.psum(gain_part, ("joint", "frame"))
    upper = normed_grad * norm_gain
    token_grad = rinv * (upper - normed * jnp.mean(upper * normed, axis=1, keepdims=True))
    token_grad = token_grad.astype(jnp.bfloat16).reshape(local_frames, joints, width)
    back = jnp.concatenate(
        [attended.reshape(local_frames, joints, inner), token_grad], axis=2
    ).transpose(1, 0, 2)
    back = lax.all_to_all(back, "joint", 0, 1, tiled=True)
    attended_out = back[:, :, :inner]
    token_out = back[:, :, inner:]
    return (attended_out, token_out, weight_grad, gain_grad)


def solution(mesh):
    placed = (P("joint", "frame", None), P(), P("frame", None), P("joint", "frame", None))
    return jax.shard_map(
        per_device_body,
        mesh=mesh,
        in_specs=placed,
        out_specs=(P("joint", "frame", None), P("joint", "frame", None), P("frame", None), P()),
        check_vma=False,
    )
```

```python
import math

import jax
import jax.numpy as jnp
from jax import lax
from jax.sharding import PartitionSpec as P


HEADS = 8
HDIM = 128


EPSILON = 1e-05


def attention_local(queries, keys_all, values_all, upstream, inv_root, groups):
    scores = (
        jnp.einsum("fihd,fjhd->fhij", queries, keys_all, preferred_element_type=jnp.float32)
        * inv_root
    )
    probs = jax.nn.softmax(scores, axis=-1)
    probs_low = probs.astype(jnp.bfloat16)
    attended = jnp.einsum(
        "fhij,fjhd->fihd", probs_low, values_all, preferred_element_type=jnp.float32
    ).astype(jnp.bfloat16)
    prob_grad = jnp.einsum(
        "fihd,fjhd->fhij", upstream, values_all, preferred_element_type=jnp.float32
    )
    carried = jnp.sum(probs * prob_grad, axis=-1, keepdims=True)
    score_grad = (probs * (prob_grad - carried) * inv_root).astype(jnp.bfloat16)
    query_grad = jnp.einsum(
        "fhij,fjhd->fihd", score_grad, keys_all, preferred_element_type=jnp.float32
    ).astype(jnp.bfloat16)
    frames, joints = queries.shape[0], queries.shape[1]
    size = joints // groups
    sg = score_grad.reshape(frames, HEADS, groups, size, joints)
    pl_ = probs_low.reshape(frames, HEADS, groups, size, joints)
    qg = queries.reshape(frames, groups, size, HEADS, HDIM)
    ug = upstream.reshape(frames, groups, size, HEADS, HDIM)
    key_part = jnp.einsum("fhgij,fgihd->fgjhd", sg, qg, preferred_element_type=jnp.float32)
    value_part = jnp.einsum("fhgij,fgihd->fgjhd", pl_, ug, preferred_element_type=jnp.float32)
    key_grad = jnp.sum(key_part.astype(jnp.bfloat16).astype(jnp.float32), axis=1).astype(jnp.bfloat16)
    value_grad = jnp.sum(value_part.astype(jnp.bfloat16).astype(jnp.float32), axis=1).astype(
        jnp.bfloat16
    )
    return attended, query_grad, key_grad, value_grad


def per_device_body(tokens, norm_gain, qkv_weight, out_grad):
    joint_rows, frame_rows, width = tokens.shape
    inner = out_grad.shape[2]
    joint_count = lax.axis_size("joint")
    total_tokens = joint_rows * frame_rows * joint_count * lax.axis_size("frame")
    grad_scale = 1.0 / math.sqrt(total_tokens)
    inv_root = 1.0 / math.sqrt(HDIM)
    joints = joint_rows * joint_count
    local_frames = frame_rows // joint_count
    count = joints * local_frames

    whole = lax.all_gather(qkv_weight, "frame", axis=0, tiled=True)

    packed = jnp.concatenate([tokens, out_grad], axis=2)
    packed = lax.all_to_all(packed, "joint", 1, 0, tiled=True)
    packed = packed.transpose(1, 0, 2)
    flat = packed[:, :, :width].reshape(count, width).astype(jnp.float32)
    upstream = packed[:, :, width:].reshape(local_frames, joints, HEADS, HDIM)

    rinv = lax.rsqrt(jnp.mean(flat * flat, axis=1, keepdims=True) + EPSILON)
    normed = flat * rinv
    scaled = (normed * norm_gain).astype(jnp.bfloat16)
    projected = jnp.dot(scaled, whole, preferred_element_type=jnp.float32).astype(jnp.bfloat16)
    projected = projected.reshape(local_frames, joints, 3, HEADS, HDIM)
    queries = projected[:, :, 0]
    keys_all = projected[:, :, 1]
    values_all = projected[:, :, 2]
    attended, query_grad, key_grad, value_grad = attention_local(
        queries, keys_all, values_all, upstream, inv_root, joint_count
    )
    qkv_grad = jnp.concatenate(
        [
            query_grad.reshape(count, inner),
            key_grad.reshape(count, inner),
            value_grad.reshape(count, inner),
        ],
        axis=1,
    )
    product = lax.dot_general(
        scaled, qkv_grad, (((0,), (0,)), ((), ())), preferred_element_type=jnp.float32
    )
    frame_sum = lax.psum_scatter(
        (product * grad_scale).astype(jnp.bfloat16), "frame", scatter_dimension=0, tiled=True
    )
    gathered = lax.all_gather(frame_sum, "joint", axis=0)
    weight_grad = jnp.sum(gathered.astype(jnp.float32), axis=0)
    normed_grad = lax.dot_general(
        qkv_grad, whole, (((1,), (1,)), ((), ())), preferred_element_type=jnp.float32
    )
    gain_part = jnp.sum(normed_grad * normed, axis=0) * grad_scale
    gain_grad = lax.psum(gain_part, ("joint", "frame"))
    upper = normed_grad * norm_gain
    token_grad = rinv * (upper - normed * jnp.mean(upper * normed, axis=1, keepdims=True))
    token_grad = token_grad.astype(jnp.bfloat16).reshape(local_frames, joints, width)
    back = jnp.concatenate(
        [attended.reshape(local_frames, joints, inner), token_grad], axis=2
    ).transpose(1, 0, 2)
    back = lax.all_to_all(back, "joint", 0, 1, tiled=True)
    attended_out = back[:, :, :inner]
    token_out = back[:, :, inner:]
    return (attended_out, token_out, weight_grad, gain_grad)


def solution(mesh):
    placed = (P("joint", "frame", None), P(), P("frame", None), P("joint", "frame", None))
    return jax.shard_map(
        per_device_body,
        mesh=mesh,
        in_specs=placed,
        out_specs=(P("joint", "frame", None), P("joint", "frame", None), P("frame", None), P()),
        check_vma=False,
    )
```
